256 devices in a mesh: ctx: 16 (over y_lo, z), dp: 16 (over x, y_hi, core).
Axes of the slice: x: 4, y: 4 (y_hi: 2, y_lo: 2; y = y_hi * 2 + y_lo), z: 8, core: 2. Of those that a mesh axis runs over, the one named last changes fastest.
Arguments:
- queries: bfloat16 [16, 4096, 2048], P('dp', 'ctx'), may hold values from -9 to 9, as said below
- keys: bfloat16 [16, 4096, 512], P('dp', 'ctx'), may hold values from -9 to 9
- values: bfloat16 [16, 4096, 512], P('dp', 'ctx'), may hold values from -20 to 20
- hyena_x1: bfloat16 [16, 4096, 2048], P('dp', 'ctx'), may hold values from -6 to 6
- hyena_x2: bfloat16 [16, 4096, 2048], P('dp', 'ctx'), may hold values from -6 to 6
- hyena_v: bfloat16 [16, 4096, 2048], P('dp', 'ctx'), may hold values from -6 to 6
- filters: bfloat16 [128, 128], replicated, may hold values from -6 to 6
- panels: bfloat16 [16, 512, 4096], P('dp', 'ctx'), may hold values from -6 to 6
- owner: int32 [16, 512, 1], P('dp', 'ctx'), may hold values from 0 to 15; in each aligned block of 32 rows (0 to 31, 32 to 63, ..., all dimensions but the last counted through in order) at most 8 rows name the same one
- step_rows: int32 [16, 512], P('dp', 'ctx'), may hold values from 0 to 4095, as said below
Outputs:
- mixed: bfloat16 [16, 4096, 2048], P('dp', 'ctx')
The draws below stay inside these ranges and needn't reach their ends.
Inputs may be any that keep to these rules, and one draw needn't show every extreme that they name: In the hidden draw a few queries are aligned with two earlier keys; the normal draw stays within 6. `step_rows`: the panels held by the device at index c of ctx belong to positions c * 256 to (c + 1) * 256 - 1 of their traces. Of the panels on one device, at most 8 have the same owner, and that bound is reached.
All inputs are finite; a program needn't handle non-finite values.
Results may differ from the reference program's by a relative error of at most 0.0055.
Values may be sent and summed in bfloat16 or wider, within the bound.
No kernel may reach another device: no remote copies, remote signals or barrier semaphores. Data moves between devices by JAX's collectives and lax.ppermute only.
A program may use at most 128 MiB of HBM per device.

```python
import math
import jax
import jax.numpy as jnp
import numpy as np
from jax import lax

HEADS = 16
KV_HEADS = 4
HEAD_DIM = 128
TAPS = 128
GROUP = 16
TOK_DEV = 256
PAN_DEV = 32
CHANNELS = 2048
FGROUPS = 128
HINT = 4096
SEQ = 4096
TRACES = 16
PANELS = 512
CAP = 8
N_DP = 16


def base_values(key, shape):
    return jnp.clip(jax.random.normal(key, shape, jnp.float32), -6.0, 6.0)


def draw_queries(key, part):
    base = base_values(jax.random.fold_in(key, 1), (TRACES, SEQ, HEADS * HEAD_DIM))
    return base.astype(jnp.bfloat16)


def draw_keys(key, part):
    base = base_values(jax.random.fold_in(key, 2), (TRACES, SEQ, KV_HEADS * HEAD_DIM))
    return base.astype(jnp.bfloat16)


def draw_filters(key, part):
    span = jnp.exp(jax.random.uniform(jax.random.fold_in(key, 3), (FGROUPS, 1), jnp.float32, math.log(8.0), math.log(1000.0)))
    rate = jnp.exp(-1.0 / span)
    norm = jnp.sqrt((1.0 - rate ** (2 * TAPS)) / (1.0 - rate * rate))
    lags = jnp.arange(TAPS, dtype=jnp.float32)[None, :]
    noise = base_values(jax.random.fold_in(key, 4), (FGROUPS, TAPS))
    return (noise * rate ** lags / norm).astype(jnp.bfloat16)


def draw_step_rows(key, part):
    offset = jax.random.randint(jax.random.fold_in(key, 5), (TRACES, PANELS), 0, TOK_DEV)
    within = jnp.arange(PANELS, dtype=jnp.int32) % PAN_DEV
    offset = jnp.where(within[None, :] == 0, TOK_DEV - 1, jnp.where(within[None, :] == 1, 0, offset))
    shard = jnp.arange(PANELS, dtype=jnp.int32) // PAN_DEV
    return (shard * TOK_DEV)[None, :] + offset


def levels(own_key, extent, split, low, high):
    def one(axis_at, blocks):
        draws = jax.random.uniform(jax.random.fold_in(jax.random.fold_in(own_key, 6), axis_at), (blocks,), jnp.float32, low / len(split), high / len(split))
        return jnp.repeat(jnp.exp(draws), extent[axis_at] // blocks).reshape((-1,) + (1,) * (len(extent) - axis_at - 1))

    gain = one(*split[0])
    for cut in split[1:]:
        gain = gain * one(*cut)
    return gain


def routed_block(rng, own, number, rows, amount, top, reach, skew):
    order = jax.random.permutation(rng, amount)
    packed, common = load_shares(amount, rows * top, reach, skew, True), load_shares(amount, rows * top, reach, skew, False)
    places = jnp.arange(amount)

    def named(sizes, turn):
        used = int((sizes > 0).sum())
        fixed = max(1, used // 4)
        moved = fixed + (places - fixed + turn * (used - fixed)) % max(1, amount - fixed)
        return jnp.zeros((amount,), jnp.int32).at[order[jnp.where(places < fixed, places, moved)]].set(jnp.asarray(sizes, jnp.int32))

    sizes = jnp.where(number % 4 == 0, named(packed, number // 4), named(common, number - number // 4 - 1))
    mixed = jax.random.permutation(jax.random.fold_in(own, 3), amount)
    donor, sink = mixed[0:amount // 2 * 2:2], mixed[1:amount // 2 * 2:2]
    margin = jnp.minimum(sizes[donor] - 1, reach - sizes[sink]) // 2
    margin = jnp.where((donor == order[0]) | (sink == order[0]) | (sizes[sink] == 0), 0, jnp.maximum(margin, 0))
    moved = jax.random.randint(jax.random.fold_in(own, 4), (amount // 2,), 0, 1 << 20) % (margin + 1)
    sizes = sizes.at[donor].add(-moved).at[sink].add(moved)
    labels = jnp.searchsorted(jnp.cumsum(sizes), jnp.arange(rows * top), side="right").astype(jnp.int32)
    table = labels.reshape(top, rows).T
    table = table[jax.random.permutation(jax.random.fold_in(own, 1), rows)]
    turn = jax.random.randint(jax.random.fold_in(own, 2), (rows, 1), 0, top)
    return jnp.take_along_axis(table, (jnp.arange(top)[None, :] + turn) % top, axis=1)


def load_shares(count, total, most, lean, full):
    weights = [(1 << 20) // math.isqrt(grade ** lean) + 1 for grade in range(1, count + 1)]
    largest = most if full else min(most, max(-(-total // count), total * weights[0] // sum(weights)))
    least = 1 if total - largest >= count - 1 else 0
    given, spare = [largest] + [least] * (count - 1), total - largest - least * (count - 1)
    while spare > 0:
        movable = [i for i in range(1, count) if given[i] < largest] or [i for i in range(1, count) if given[i] < most]
        whole, budget = sum([weights[i] for i in movable]), spare
        for i in movable:
            more = min(most - given[i], max(1, budget * weights[i] // whole), spare)
            given[i] = given[i] + more
            spare = spare - more
    return np.array(given)


def gaussian(own_key, shape, spread, most, cuts=(), kind=jnp.bfloat16):
    entries = spread * jax.random.normal(own_key, shape, jnp.float32)
    if cuts:
        entries = entries * levels(own_key, shape, cuts, -0.22, 0.18)
    return jnp.clip(entries, -most, most).astype(kind)


def setup_inputs(seed: int = 0) -> dict:
    key_of = jax.random.split(jax.random.key(seed), 11)
    queries = draw_queries(jax.random.fold_in(key_of[10], 71), 0)
    keys = draw_keys(jax.random.fold_in(key_of[10], 71), 0)
    values = gaussian(key_of[2], (TRACES, SEQ, KV_HEADS * HEAD_DIM), 4.0, 20.0, ((0, 16), (1, 16)))
    hyena_x1 = gaussian(key_of[3], (TRACES, SEQ, CHANNELS), 1.0, 6.0, ((0, 16), (1, 16)))
    hyena_x2 = gaussian(key_of[4], (TRACES, SEQ, CHANNELS), 1.0, 6.0, ((0, 16), (1, 16)))
    hyena_v = gaussian(key_of[5], (TRACES, SEQ, CHANNELS), 1.0, 6.0, ((0, 16), (1, 16)))
    filters = draw_filters(jax.random.fold_in(key_of[10], 71), 0)
    panels = gaussian(key_of[7], (TRACES, PANELS, HINT), 1.0, 6.0, ((0, 16), (1, 16)))
    owner_keys = jax.random.split(jax.random.fold_in(key_of[8], 1), TRACES * PANELS // PAN_DEV)
    owner_turns = jax.random.permutation(jax.random.fold_in(key_of[8], 3), TRACES * PANELS // PAN_DEV)
    owner = jax.vmap(lambda own, number: routed_block(jax.random.fold_in(key_of[8], 2), own, number, PAN_DEV, N_DP, 1, CAP, 2))(owner_keys, owner_turns).reshape((TRACES, PANELS, 1))
    step_rows = draw_step_rows(jax.random.fold_in(key_of[10], 71), 0)
    return dict(queries=queries, keys=keys, values=values, hyena_x1=hyena_x1, hyena_x2=hyena_x2, hyena_v=hyena_v, filters=filters, panels=panels, owner=owner, step_rows=step_rows)


NEG = -1e30


def conv_trace(u_rows, filters):
    width = u_rows.shape[1]
    nblk = SEQ // TAPS
    ext = jnp.concatenate([jnp.zeros((TAPS, width), jnp.float32), u_rows.astype(jnp.float32)], 0)
    blocks = ext.reshape(nblk + 1, TAPS, FGROUPS, GROUP)
    lag = jnp.arange(TAPS, dtype=jnp.int32)[:, None] - jnp.arange(TAPS, dtype=jnp.int32)[None, :]
    taps_f = filters.astype(jnp.float32)
    lower = jnp.where(lag >= 0, taps_f[:, jnp.clip(lag, 0, TAPS - 1)], jnp.float32(0.0))
    upper = jnp.where(lag < 0, taps_f[:, jnp.clip(lag + TAPS, 0, TAPS - 1)], jnp.float32(0.0))
    hi = lax.Precision.HIGHEST
    conv = jnp.einsum("gij,bjgc->bigc", lower, blocks[1:], precision=hi)
    conv = conv + jnp.einsum("gij,bjgc->bigc", upper, blocks[:-1], precision=hi)
    return conv.reshape(SEQ, width)


def attend_trace(q_rows, k_rows, v_rows):
    grp = HEADS // KV_HEADS
    qblk = math.gcd(SEQ, 512)
    scale = HEAD_DIM ** -0.5
    k_f = k_rows.astype(jnp.float32).reshape(SEQ, KV_HEADS, HEAD_DIM)
    v_f = v_rows.astype(jnp.float32).reshape(SEQ, KV_HEADS, HEAD_DIM)
    q_blocks = q_rows.reshape(SEQ // qblk, qblk, KV_HEADS, grp, HEAD_DIM)
    key_pos = jnp.arange(SEQ, dtype=jnp.int32)
    hi = lax.Precision.HIGHEST

    def one_block(item):
        index, q_blk = item
        scores = jnp.einsum("rhgd,khd->hgrk", q_blk.astype(jnp.float32), k_f, precision=hi) * scale
        q_pos = index * qblk + jnp.arange(qblk, dtype=jnp.int32)
        allowed = key_pos[None, :] <= q_pos[:, None]
        scores = jnp.where(allowed, scores, NEG)
        top = jnp.max(scores, axis=-1)
        expo = jnp.where(allowed, jnp.exp(scores - top[..., None]), jnp.float32(0.0))
        total = jnp.sum(expo, axis=-1)
        weight = expo.astype(jnp.bfloat16).astype(jnp.float32)
        numer = jnp.einsum("hgrk,khd->hgrd", weight, v_f, precision=hi)
        out = numer / total[..., None]
        return out.transpose(2, 0, 1, 3).reshape(qblk, HEADS * HEAD_DIM)

    outs = lax.map(one_block, (jnp.arange(SEQ // qblk, dtype=jnp.int32), q_blocks))
    return outs.reshape(SEQ, HEADS * HEAD_DIM)


def reference(queries, keys, values, hyena_x1, hyena_x2, hyena_v, filters, panels, owner, step_rows):
    def one_trace(item):
        q_rows, k_rows, v_rows, first, second, third = item
        u_rows = (first.astype(jnp.float32) * third.astype(jnp.float32)).astype(jnp.bfloat16)
        hyena = second.astype(jnp.float32) * conv_trace(u_rows, filters)
        return hyena + attend_trace(q_rows, k_rows, v_rows)

    mixed = lax.map(one_trace, (queries, keys, values, hyena_x1, hyena_x2, hyena_v))
    gates = panels[:, :, :CHANNELS].astype(jnp.float32)
    vals = panels[:, :, CHANNELS:].astype(jnp.float32)
    hint = (jax.nn.sigmoid(gates) * vals).astype(jnp.bfloat16).astype(jnp.float32)
    mixed = mixed.at[owner[:, :, 0], step_rows].add(hint)
    return mixed.astype(jnp.bfloat16)
```

```python
import math

import jax
import jax.numpy as jnp
from jax import lax
from jax.sharding import PartitionSpec as P
from jax.experimental import pallas as pl
from jax.experimental.pallas import tpu as pltpu

HEADS = 16
KV_HEADS = 4
HEAD_DIM = 128


NEG = -1e30


def passed_along(block, axis, distance):
    devices = range(lax.axis_size(axis))
    route = [(i - distance, i) for i in devices if i - distance in devices]
    return lax.ppermute(block, axis, route)


def flash_kernel(c_ref, q_ref, k_ref, v_ref, o_ref, m_sc, l_sc, acc_sc):
    d = pl.program_id(1)
    last = pl.num_programs(1) - 1
    c = c_ref[0]
    grp = HEADS // KV_HEADS
    tok = q_ref.shape[0]
    scale = HEAD_DIM ** (-0.5)

    @pl.when(d == 0)
    def _():
        m_sc[...] = jnp.full_like(m_sc, NEG)
        l_sc[...] = jnp.zeros_like(l_sc)
        acc_sc[...] = jnp.zeros_like(acc_sc)

    @pl.when(d <= c)
    def _():
        q = q_ref[...]
        qs = jnp.concatenate(
            [q[:, j * HEAD_DIM : (j + 1) * HEAD_DIM] for j in range(grp)], axis=0
        )
        k = k_ref[0]
        v = v_ref[0]
        s = lax.dot_general(
            qs, k, (((1,), (1,)), ((), ())), preferred_element_type=jnp.float32
        ) * scale
        rows = lax.broadcasted_iota(jnp.int32, s.shape, 0) % tok
        cols = lax.broadcasted_iota(jnp.int32, s.shape, 1)
        allowed = (cols <= rows) | (d > 0)
        s = jnp.where(allowed, s, NEG)
        m_old = m_sc[...]
        m_new = jnp.maximum(m_old, jnp.max(s, axis=-1, keepdims=True))
        p = jnp.exp(s - m_new)
        alpha = jnp.exp(m_old - m_new)
        l_sc[...] = alpha * l_sc[...] + jnp.sum(p, axis=-1, keepdims=True)
        acc_sc[...] = alpha * acc_sc[...] + jnp.dot(
            p.astype(jnp.bfloat16), v, preferred_element_type=jnp.float32
        )
        m_sc[...] = m_new

    @pl.when(d == last)
    def _():
        for j in range(grp):
            rows_j = slice(j * tok, (j + 1) * tok)
            o_ref[:, j * HEAD_DIM : (j + 1) * HEAD_DIM] = acc_sc[rows_j] / l_sc[rows_j]


def flash(ctx_index, query, kv_stack):
    tok = query.shape[0]
    nblk = kv_stack.shape[0]
    grp = HEADS // KV_HEADS
    width = grp * HEAD_DIM

    def q_map(g, d, c):
        return (0, g)

    def k_map(g, d, c):
        return (jnp.minimum(d, c[0]), 0, g)

    def v_map(g, d, c):
        return (jnp.minimum(d, c[0]), 0, KV_HEADS + g)

    return pl.pallas_call(
        flash_kernel,
        out_shape=jax.ShapeDtypeStruct((tok, HEADS * HEAD_DIM), jnp.float32),
        grid_spec=pltpu.PrefetchScalarGridSpec(
            num_scalar_prefetch=1,
            grid=(KV_HEADS, nblk),
            in_specs=[
                pl.BlockSpec((tok, width), q_map),
                pl.BlockSpec((1, tok, HEAD_DIM), k_map),
                pl.BlockSpec((1, tok, HEAD_DIM), v_map),
            ],
            out_specs=pl.BlockSpec((tok, width), q_map),
            scratch_shapes=[
                pltpu.VMEM((grp * tok, 1), jnp.float32),
                pltpu.VMEM((grp * tok, 1), jnp.float32),
                pltpu.VMEM((grp * tok, HEAD_DIM), jnp.float32),
            ],
        ),
        compiler_params=pltpu.CompilerParams(
            dimension_semantics=("arbitrary", "arbitrary")
        ),
    )(jnp.reshape(ctx_index, (1,)).astype(jnp.int32), query, kv_stack, kv_stack)


def attention(query, key_rows, val_rows, tok, ctx_index):
    count = lax.axis_size("ctx")
    kv = jnp.concatenate([key_rows, val_rows], axis=1)
    pieces = [kv]
    for dist in range(1, count):
        pieces.append(passed_along(kv, "ctx", dist))
    kv_stack = jnp.stack(pieces, axis=0)
    return flash(ctx_index, query, kv_stack)


def hyena_conv(first_in, value_in, filters, tok):
    width = first_in.shape[1]
    taps = filters.shape[1]
    fgroups = filters.shape[0]
    u_rows = (first_in.astype(jnp.float32) * value_in.astype(jnp.float32)).astype(jnp.bfloat16)
    before = passed_along(u_rows[tok - taps :], "ctx", 1)
    extended = jnp.concatenate([before, u_rows], 0)
    nblk = tok // taps
    blocks = extended.reshape(nblk + 1, taps, fgroups, width // fgroups)
    rows_at = jnp.arange(taps, dtype=jnp.int32)
    lag = rows_at[:, None] - rows_at[None, :]
    wrapped = (lag + taps) % taps
    selector = (wrapped[None, :, :] == rows_at[:, None, None]).astype(jnp.bfloat16)
    circulant = jnp.einsum(
        "gk,kij->gij", filters, selector, preferred_element_type=jnp.float32
    ).astype(jnp.bfloat16)
    nothing = jnp.zeros((), jnp.bfloat16)
    lower = jnp.where((lag >= 0)[None], circulant, nothing)
    upper = jnp.where((lag < 0)[None], circulant, nothing)
    conv = jnp.einsum("gij,bjgc->bigc", lower, blocks[1:], preferred_element_type=jnp.float32)
    conv = conv + jnp.einsum(
        "gij,bjgc->bigc", upper, blocks[:-1], preferred_element_type=jnp.float32
    )
    return conv.reshape(tok, width)


def blend(rows, width):
    gates = rows[:, :width].astype(jnp.float32)
    vals = rows[:, width:].astype(jnp.float32)
    return (jax.nn.sigmoid(gates) * vals).astype(jnp.bfloat16)


def place_rows(slots, rows, total_slots):
    placing = (jnp.arange(total_slots, dtype=jnp.int32)[:, None] == slots[None, :]).astype(
        jnp.bfloat16
    )
    return jnp.dot(placing, rows, preferred_element_type=jnp.float32).astype(jnp.bfloat16)


def route_hints(panels, owner, step_rows, width, tok, ctx_index):
    dp_count = lax.axis_size("dp")
    count = panels.shape[1]
    entries = panels.shape[2]
    cap = min(count, 4 * count // dp_count)
    owners = owner[0, :, 0]
    marks = (owners[:, None] == jnp.arange(dp_count, dtype=jnp.int32)[None, :]).astype(jnp.int32)
    before_mask = (
        jnp.arange(count, dtype=jnp.int32)[:, None] > jnp.arange(count, dtype=jnp.int32)[None, :]
    ).astype(jnp.int32)
    earlier = jnp.sum(jnp.dot(before_mask, marks) * marks, axis=1)
    slots = owners * cap + earlier
    base_row = ctx_index * tok
    row_buffer = jnp.full((dp_count * cap,), base_row, jnp.int32).at[slots].set(step_rows[0])
    arrived_rows = (
        lax.all_to_all(
            row_buffer.reshape(dp_count, cap), "dp", split_axis=0, concat_axis=0, tiled=True
        ).reshape(dp_count * cap)
        - base_row
    )
    buffer = place_rows(slots, panels[0], dp_count * cap)
    received = lax.all_to_all(
        buffer.reshape(dp_count, cap, entries), "dp", split_axis=0, concat_axis=0, tiled=True
    )
    arrived = blend(received.reshape(dp_count * cap, entries), width)
    landing = (jnp.arange(tok, dtype=jnp.int32)[:, None] == arrived_rows[None, :]).astype(
        jnp.bfloat16
    )
    return jnp.dot(landing, arrived, preferred_element_type=jnp.float32)


def per_device(
    queries, keys, values, hyena_x1, hyena_x2, hyena_v, filters, panels, owner, step_rows
):
    tok = queries.shape[1]
    width = hyena_x1.shape[2]
    ctx_index = lax.axis_index("ctx")
    conv = hyena_conv(hyena_x1[0], hyena_v[0], filters, tok)
    attended = attention(queries[0], keys[0], values[0], tok, ctx_index)
    hints = route_hints(panels, owner, step_rows, width, tok, ctx_index)
    total = hyena_x2[0].astype(jnp.float32) * conv + attended + hints
    return total.astype(jnp.bfloat16)[None]


def solution(mesh):
    placed = (
        P("dp", "ctx", None),
        P("dp", "ctx", None),
        P("dp", "ctx", None),
        P("dp", "ctx", None),
        P("dp", "ctx", None),
        P("dp", "ctx", None),
        P(),
        P("dp", "ctx", None),
        P("dp", "ctx", None),
        P("dp", "ctx"),
    )
    return jax.shard_map(
        per_device, mesh=mesh, in_specs=placed, out_specs=P("dp", "ctx", None), check_vma=False
    )
```

```python
import math

import jax
import jax.numpy as jnp
from jax import lax
from jax.sharding import PartitionSpec as P
from jax.experimental import pallas as pl
from jax.experimental.pallas import tpu as pltpu

HEADS = 16
KV_HEADS = 4
HEAD_DIM = 128


NEG = -1e30


def passed_along(block, axis, distance):
    devices = range(lax.axis_size(axis))
    route = [(i - distance, i) for i in devices if i - distance in devices]
    return lax.ppermute(block, axis, route)


def flash_kernel(c_ref, q_ref, kv_ref, o_ref, qs_sc, m_sc, l_sc, acc_sc):
    d = pl.program_id(0)
    last = pl.num_programs(0) - 1
    c = c_ref[0]
    grp = HEADS // KV_HEADS
    tok = q_ref.shape[0]
    scale = HEAD_DIM ** (-0.5)

    @pl.when(d == 0)
    def _():
        for g in range(KV_HEADS):
            for j in range(grp):
                col = (g * grp + j) * HEAD_DIM
                qs_sc[g, j * tok : (j + 1) * tok, :] = q_ref[:, col : col + HEAD_DIM]
        m_sc[...] = jnp.full_like(m_sc, NEG)
        l_sc[...] = jnp.zeros_like(l_sc)
        acc_sc[...] = jnp.zeros_like(acc_sc)

    def update(masked):
        for g in range(KV_HEADS):
            k = kv_ref[0, :, g * HEAD_DIM : (g + 1) * HEAD_DIM]
            v = kv_ref[0, :, (KV_HEADS + g) * HEAD_DIM : (KV_HEADS + g + 1) * HEAD_DIM]
            s = lax.dot_general(
                k, qs_sc[g], (((1,), (1,)), ((), ())), preferred_element_type=jnp.float32
            ) * scale
            if masked:
                rows = lax.broadcasted_iota(jnp.int32, s.shape, 0)
                cols = lax.broadcasted_iota(jnp.int32, s.shape, 1) % tok
                s = jnp.where(rows <= cols, s, NEG)
            m_old = m_sc[g]
            m_new = jnp.maximum(m_old, jnp.max(s, axis=0, keepdims=True))
            p = jnp.exp(s - m_new)
            alpha = jnp.exp(m_old - m_new)
            l_sc[g] = alpha * l_sc[g] + jnp.sum(p, axis=0, keepdims=True)
            pv = lax.dot_general(
                v, p.astype(jnp.bfloat16), (((0,), (0,)), ((), ())),
                preferred_element_type=jnp.float32,
            )
            acc_sc[g] = alpha * acc_sc[g] + pv
            m_sc[g] = m_new

    @pl.when(d == 0)
    def _():
        update(True)

    @pl.when((d > 0) & (d <= c))
    def _():
        update(False)

    @pl.when(d == last)
    def _():
        for g in range(KV_HEADS):
            normed = acc_sc[g] / l_sc[g]
            for j in range(grp):
                col = (g * grp + j) * HEAD_DIM
                o_ref[:, col : col + HEAD_DIM] = normed[:, j * tok : (j + 1) * tok].T


def flash(ctx_index, query, kv_stack):
    tok = query.shape[0]
    nblk = kv_stack.shape[0]
    grp = HEADS // KV_HEADS

    def q_map(d, c):
        return (0, 0)

    def kv_map(d, c):
        return (jnp.minimum(d, c[0]), 0, 0)

    return pl.pallas_call(
        flash_kernel,
        out_shape=jax.ShapeDtypeStruct((tok, HEADS * HEAD_DIM), jnp.float32),
        grid_spec=pltpu.PrefetchScalarGridSpec(
            num_scalar_prefetch=1,
            grid=(nblk,),
            in_specs=[
                pl.BlockSpec((tok, HEADS * HEAD_DIM), q_map),
                pl.BlockSpec((1, tok, 2 * KV_HEADS * HEAD_DIM), kv_map),
            ],
            out_specs=pl.BlockSpec((tok, HEADS * HEAD_DIM), q_map),
            scratch_shapes=[
                pltpu.VMEM((KV_HEADS, grp * tok, HEAD_DIM), jnp.bfloat16),
                pltpu.VMEM((KV_HEADS, 1, grp * tok), jnp.float32),
                pltpu.VMEM((KV_HEADS, 1, grp * tok), jnp.float32),
                pltpu.VMEM((KV_HEADS, HEAD_DIM, grp * tok), jnp.float32),
            ],
        ),
        compiler_params=pltpu.CompilerParams(dimension_semantics=("arbitrary",)),
    )(jnp.reshape(ctx_index, (1,)).astype(jnp.int32), query, kv_stack)


def attention(query, key_rows, val_rows, tok, ctx_index):
    count = lax.axis_size("ctx")
    kv = jnp.concatenate([key_rows, val_rows], axis=1)
    pieces = [kv]
    for dist in range(1, count):
        pieces.append(passed_along(kv, "ctx", dist))
    kv_stack = jnp.stack(pieces, axis=0)
    return flash(ctx_index, query, kv_stack)


def hyena_conv(first_in, value_in, filters, tok):
    width = first_in.shape[1]
    taps = filters.shape[1]
    fgroups = filters.shape[0]
    u_rows = (first_in.astype(jnp.float32) * value_in.astype(jnp.float32)).astype(jnp.bfloat16)
    before = passed_along(u_rows[tok - taps :], "ctx", 1)
    extended = jnp.concatenate([before, u_rows], 0)
    nblk = tok // taps
    blocks = extended.reshape(nblk + 1, taps, fgroups, width // fgroups)
    rows_at = jnp.arange(taps, dtype=jnp.int32)
    lag = rows_at[:, None] - rows_at[None, :]
    wrapped = (lag + taps) % taps
    selector = (wrapped[None, :, :] == rows_at[:, None, None]).astype(jnp.bfloat16)
    circulant = jnp.einsum(
        "gk,kij->gij", filters, selector, preferred_element_type=jnp.float32
    ).astype(jnp.bfloat16)
    nothing = jnp.zeros((), jnp.bfloat16)
    lower = jnp.where((lag >= 0)[None], circulant, nothing)
    upper = jnp.where((lag < 0)[None], circulant, nothing)
    conv = jnp.einsum("gij,bjgc->bigc", lower, blocks[1:], preferred_element_type=jnp.float32)
    conv = conv + jnp.einsum(
        "gij,bjgc->bigc", upper, blocks[:-1], preferred_element_type=jnp.float32
    )
    return conv.reshape(tok, width)


def blend(rows, width):
    gates = rows[:, :width].astype(jnp.float32)
    vals = rows[:, width:].astype(jnp.float32)
    return (jax.nn.sigmoid(gates) * vals).astype(jnp.bfloat16)


def place_rows(slots, rows, total_slots):
    placing = (jnp.arange(total_slots, dtype=jnp.int32)[:, None] == slots[None, :]).astype(
        jnp.bfloat16
    )
    return jnp.dot(placing, rows, preferred_element_type=jnp.float32).astype(jnp.bfloat16)


def route_hints(panels, owner, step_rows, width, tok, ctx_index):
    dp_count = lax.axis_size("dp")
    count = panels.shape[1]
    entries = panels.shape[2]
    cap = min(count, 4 * count // dp_count)
    owners = owner[0, :, 0]
    marks = (owners[:, None] == jnp.arange(dp_count, dtype=jnp.int32)[None, :]).astype(jnp.int32)
    before_mask = (
        jnp.arange(count, dtype=jnp.int32)[:, None] > jnp.arange(count, dtype=jnp.int32)[None, :]
    ).astype(jnp.int32)
    earlier = jnp.sum(jnp.dot(before_mask, marks) * marks, axis=1)
    slots = owners * cap + earlier
    base_row = ctx_index * tok
    row_buffer = jnp.full((dp_count * cap,), base_row, jnp.int32).at[slots].set(step_rows[0])
    arrived_rows = (
        lax.all_to_all(
            row_buffer.reshape(dp_count, cap), "dp", split_axis=0, concat_axis=0, tiled=True
        ).reshape(dp_count * cap)
        - base_row
    )
    buffer = place_rows(slots, panels[0], dp_count * cap)
    received = lax.all_to_all(
        buffer.reshape(dp_count, cap, entries), "dp", split_axis=0, concat_axis=0, tiled=True
    )
    arrived = blend(received.reshape(dp_count * cap, entries), width)
    landing = (jnp.arange(tok, dtype=jnp.int32)[:, None] == arrived_rows[None, :]).astype(
        jnp.bfloat16
    )
    return jnp.dot(landing, arrived, preferred_element_type=jnp.float32)


def per_device(
    queries, keys, values, hyena_x1, hyena_x2, hyena_v, filters, panels, owner, step_rows
):
    tok = queries.shape[1]
    width = hyena_x1.shape[2]
    ctx_index = lax.axis_index("ctx")
    conv = hyena_conv(hyena_x1[0], hyena_v[0], filters, tok)
    attended = attention(queries[0], keys[0], values[0], tok, ctx_index)
    hints = route_hints(panels, owner, step_rows, width, tok, ctx_index)
    total = hyena_x2[0].astype(jnp.float32) * conv + attended + hints
    return total.astype(jnp.bfloat16)[None]


def solution(mesh):
    placed = (
        P("dp", "ctx", None),
        P("dp", "ctx", None),
        P("dp", "ctx", None),
        P("dp", "ctx", None),
        P("dp", "ctx", None),
        P("dp", "ctx", None),
        P(),
        P("dp", "ctx", None),
        P("dp", "ctx", None),
        P("dp", "ctx"),
    )
    return jax.shard_map(
        per_device, mesh=mesh, in_specs=placed, out_specs=P("dp", "ctx", None), check_vma=False
    )
```

```python
import math

import jax
import jax.numpy as jnp
from jax import lax
from jax.sharding import PartitionSpec as P
from jax.experimental import pallas as pl
from jax.experimental.pallas import tpu as pltpu

HEADS = 16
KV_HEADS = 4
HEAD_DIM = 128


NEG = -1e30


def passed_along(block, axis, distance):
    devices = range(lax.axis_size(axis))
    route = [(i - distance, i) for i in devices if i - distance in devices]
    return lax.ppermute(block, axis, route)


ROW = 8


def flash_kernel(*refs):
    flags_ref, q_ref = refs[0], refs[1]
    count = len(refs) - 7
    kv_refs = refs[2 : 2 + count]
    o_ref, qs_sc, m_sc, l_sc, acc_sc = refs[2 + count :]
    grp = HEADS // KV_HEADS
    tok = q_ref.shape[0]
    scale = HEAD_DIM ** (-0.5)

    for g in range(KV_HEADS):
        for j in range(grp):
            col = (g * grp + j) * HEAD_DIM
            qs_sc[g, j * tok : (j + 1) * tok, :] = q_ref[:, col : col + HEAD_DIM]
    m_sc[...] = jnp.full_like(m_sc, NEG)
    l_sc[...] = jnp.zeros_like(l_sc)
    acc_sc[...] = jnp.zeros_like(acc_sc)

    def update(kv_ref, masked):
        def one(g, carry):
            k = kv_ref[g]
            v = kv_ref[KV_HEADS + g]
            s = lax.dot_general(
                k, qs_sc[g], (((1,), (1,)), ((), ())), preferred_element_type=jnp.float32
            ) * scale
            if masked:
                rows = lax.broadcasted_iota(jnp.int32, s.shape, 0)
                cols = lax.broadcasted_iota(jnp.int32, s.shape, 1) % tok
                s = jnp.where(rows <= cols, s, NEG)
            m_old = m_sc[g]
            m_new = jnp.maximum(m_old, jnp.max(s, axis=0, keepdims=True))
            p = jnp.exp(s - m_new)
            alpha = jnp.exp(m_old - m_new)
            l_sc[g] = alpha * l_sc[g] + jnp.sum(p, axis=0, keepdims=True)
            pv = lax.dot_general(
                v, p.astype(jnp.bfloat16), (((0,), (0,)), ((), ())),
                preferred_element_type=jnp.float32,
            )
            acc_sc[g] = alpha * acc_sc[g] + pv
            m_sc[g] = m_new
            return carry

        lax.fori_loop(0, KV_HEADS, one, 0)

    update(kv_refs[0], True)
    for i in range(1, count):

        @pl.when(flags_ref[i] > 0)
        def _(i=i):
            update(kv_refs[i], False)

    for g in range(KV_HEADS):
        normed = acc_sc[g] / l_sc[g]
        for j in range(grp):
            col = (g * grp + j) * HEAD_DIM
            o_ref[:, col : col + HEAD_DIM] = normed[:, j * tok : (j + 1) * tok].T


def flash(flags, query, blocks):
    tok = query.shape[0]
    grp = HEADS // KV_HEADS
    vmem = pl.BlockSpec(memory_space=pltpu.VMEM)
    return pl.pallas_call(
        flash_kernel,
        out_shape=jax.ShapeDtypeStruct((tok, HEADS * HEAD_DIM), jnp.float32),
        in_specs=[pl.BlockSpec(memory_space=pltpu.SMEM)] + [vmem] * (1 + len(blocks)),
        out_specs=vmem,
        scratch_shapes=[
            pltpu.VMEM((KV_HEADS, grp * tok, HEAD_DIM), jnp.bfloat16),
            pltpu.VMEM((KV_HEADS, 1, grp * tok), jnp.float32),
            pltpu.VMEM((KV_HEADS, 1, grp * tok), jnp.float32),
            pltpu.VMEM((KV_HEADS, HEAD_DIM, grp * tok), jnp.float32),
        ],
        compiler_params=pltpu.CompilerParams(vmem_limit_bytes=48 * 1024 * 1024),
    )(flags, query, *blocks)


def attention(query, key_rows, val_rows, tok, ctx_index):
    count = lax.axis_size("ctx")
    rows = count // ROW
    kv = jnp.concatenate([key_rows, val_rows], axis=1)
    kv = kv.reshape(tok, 2 * KV_HEADS, HEAD_DIM).transpose(1, 0, 2)
    plus = [(r * ROW + z, r * ROW + (z + 1) % ROW) for r in range(rows) for z in range(ROW)]
    minus = [(r * ROW + z, r * ROW + (z - 1) % ROW) for r in range(rows) for z in range(ROW)]
    lefts, rights = [kv], [kv]
    for _ in range(ROW // 2):
        lefts.append(lax.ppermute(lefts[-1], "ctx", plus))
    for _ in range(ROW - 1 - ROW // 2):
        rights.append(lax.ppermute(rights[-1], "ctx", minus))
    row_blocks = lefts + rights[1:]
    z = ctx_index % ROW
    r = ctx_index // ROW
    flags = [jnp.int32(1)]
    flags += [(z - k >= 0).astype(jnp.int32) for k in range(1, len(lefts))]
    flags += [(z + k >= ROW).astype(jnp.int32) for k in range(1, len(rights))]
    blocks = list(row_blocks)
    for lower in range(rows - 1):
        for upper in range(lower + 1, rows):
            up = [(lower * ROW + z2, upper * ROW + z2) for z2 in range(ROW)]
            for piece in row_blocks:
                blocks.append(lax.ppermute(piece, "ctx", up))
                flags.append((r == upper).astype(jnp.int32))
    return flash(jnp.stack(flags), query, blocks)


def hyena_conv(first_in, value_in, filters, tok):
    width = first_in.shape[1]
    taps = filters.shape[1]
    fgroups = filters.shape[0]
    u_rows = (first_in.astype(jnp.float32) * value_in.astype(jnp.float32)).astype(jnp.bfloat16)
    before = passed_along(u_rows[tok - taps :], "ctx", 1)
    extended = jnp.concatenate([before, u_rows], 0)
    nblk = tok // taps
    blocks = extended.reshape(nblk + 1, taps, fgroups, width // fgroups)
    rows_at = jnp.arange(taps, dtype=jnp.int32)
    lag = rows_at[:, None] - rows_at[None, :]
    wrapped = (lag + taps) % taps
    selector = (wrapped[None, :, :] == rows_at[:, None, None]).astype(jnp.bfloat16)
    circulant = jnp.einsum(
        "gk,kij->gij", filters, selector, preferred_element_type=jnp.float32
    ).astype(jnp.bfloat16)
    nothing = jnp.zeros((), jnp.bfloat16)
    lower = jnp.where((lag >= 0)[None], circulant, nothing)
    upper = jnp.where((lag < 0)[None], circulant, nothing)
    conv = jnp.einsum("gij,bjgc->bigc", lower, blocks[1:], preferred_element_type=jnp.float32)
    conv = conv + jnp.einsum(
        "gij,bjgc->bigc", upper, blocks[:-1], preferred_element_type=jnp.float32
    )
    return conv.reshape(tok, width)


def blend(rows, width):
    gates = rows[:, :width].astype(jnp.float32)
    vals = rows[:, width:].astype(jnp.float32)
    return (jax.nn.sigmoid(gates) * vals).astype(jnp.bfloat16)


def place_rows(slots, rows, total_slots):
    placing = (jnp.arange(total_slots, dtype=jnp.int32)[:, None] == slots[None, :]).astype(
        jnp.bfloat16
    )
    return jnp.dot(placing, rows, preferred_element_type=jnp.float32).astype(jnp.bfloat16)


def route_hints(panels, owner, step_rows, width, tok, ctx_index):
    dp_count = lax.axis_size("dp")
    count = panels.shape[1]
    entries = panels.shape[2]
    cap = min(count, 4 * count // dp_count)
    owners = owner[0, :, 0]
    marks = (owners[:, None] == jnp.arange(dp_count, dtype=jnp.int32)[None, :]).astype(jnp.int32)
    before_mask = (
        jnp.arange(count, dtype=jnp.int32)[:, None] > jnp.arange(count, dtype=jnp.int32)[None, :]
    ).astype(jnp.int32)
    earlier = jnp.sum(jnp.dot(before_mask, marks) * marks, axis=1)
    slots = owners * cap + earlier
    base_row = ctx_index * tok
    row_buffer = jnp.full((dp_count * cap,), base_row, jnp.int32).at[slots].set(step_rows[0])
    arrived_rows = (
        lax.all_to_all(
            row_buffer.reshape(dp_count, cap), "dp", split_axis=0, concat_axis=0, tiled=True
        ).reshape(dp_count * cap)
        - base_row
    )
    buffer = place_rows(slots, panels[0], dp_count * cap)
    received = lax.all_to_all(
        buffer.reshape(dp_count, cap, entries), "dp", split_axis=0, concat_axis=0, tiled=True
    )
    arrived = blend(received.reshape(dp_count * cap, entries), width)
    landing = (jnp.arange(tok, dtype=jnp.int32)[:, None] == arrived_rows[None, :]).astype(
        jnp.bfloat16
    )
    return jnp.dot(landing, arrived, preferred_element_type=jnp.float32)


def per_device(
    queries, keys, values, hyena_x1, hyena_x2, hyena_v, filters, panels, owner, step_rows
):
    tok = queries.shape[1]
    width = hyena_x1.shape[2]
    ctx_index = lax.axis_index("ctx")
    conv = hyena_conv(hyena_x1[0], hyena_v[0], filters, tok)
    attended = attention(queries[0], keys[0], values[0], tok, ctx_index)
    hints = route_hints(panels, owner, step_rows, width, tok, ctx_index)
    total = hyena_x2[0].astype(jnp.float32) * conv + attended + hints
    return total.astype(jnp.bfloat16)[None]


def solution(mesh):
    placed = (
        P("dp", "ctx", None),
        P("dp", "ctx", None),
        P("dp", "ctx", None),
        P("dp", "ctx", None),
        P("dp", "ctx", None),
        P("dp", "ctx", None),
        P(),
        P("dp", "ctx", None),
        P("dp", "ctx", None),
        P("dp", "ctx"),
    )
    return jax.shard_map(
        per_device, mesh=mesh, in_specs=placed, out_specs=P("dp", "ctx", None), check_vma=False
    )
```

```python
import functools
import math

import jax
import jax.numpy as jnp
from jax import lax
from jax.sharding import PartitionSpec as P
from jax.experimental import pallas as pl
from jax.experimental.pallas import tpu as pltpu

HEADS = 16
KV_HEADS = 4
HEAD_DIM = 128


NEG = -1e30


def passed_along(block, axis, distance):
    devices = range(lax.axis_size(axis))
    route = [(i - distance, i) for i in devices if i - distance in devices]
    return lax.ppermute(block, axis, route)


ROW = 8


def flash_kernel(first, final, count, *refs):
    flags_ref, q_ref = refs[0], refs[1]
    at = 2
    if not first:
        m_in, l_in, acc_in = refs[at : at + 3]
        at += 3
    kv_refs = refs[at : at + count]
    at += count
    outs = refs[at : at + (1 if final else 3)]
    qs_sc, m_sc, l_sc, acc_sc = refs[at + len(outs) :]
    grp = HEADS // KV_HEADS
    tok = q_ref.shape[0]
    scale = HEAD_DIM ** (-0.5)

    for g in range(KV_HEADS):
        for j in range(grp):
            col = (g * grp + j) * HEAD_DIM
            qs_sc[g, j * tok : (j + 1) * tok, :] = q_ref[:, col : col + HEAD_DIM]
    if first:
        m_sc[...] = jnp.full_like(m_sc, NEG)
        l_sc[...] = jnp.zeros_like(l_sc)
        acc_sc[...] = jnp.zeros_like(acc_sc)
    else:
        m_sc[...] = m_in[...]
        l_sc[...] = l_in[...]
        acc_sc[...] = acc_in[...]

    def update(kv_ref, masked):
        def one(g, carry):
            k = kv_ref[g]
            v = kv_ref[KV_HEADS + g]
            s = lax.dot_general(
                k, qs_sc[g], (((1,), (1,)), ((), ())), preferred_element_type=jnp.float32
            ) * scale
            if masked:
                rows = lax.broadcasted_iota(jnp.int32, s.shape, 0)
                cols = lax.broadcasted_iota(jnp.int32, s.shape, 1) % tok
                s = jnp.where(rows <= cols, s, NEG)
            m_old = m_sc[g]
            m_new = jnp.maximum(m_old, jnp.max(s, axis=0, keepdims=True))
            p = jnp.exp(s - m_new)
            alpha = jnp.exp(m_old - m_new)
            l_sc[g] = alpha * l_sc[g] + jnp.sum(p, axis=0, keepdims=True)
            pv = lax.dot_general(
                v, p.astype(jnp.bfloat16), (((0,), (0,)), ((), ())),
                preferred_element_type=jnp.float32,
            )
            acc_sc[g] = alpha * acc_sc[g] + pv
            m_sc[g] = m_new
            return carry

        lax.fori_loop(0, KV_HEADS, one, 0)

    for i in range(count):
        if first and i == 0:
            update(kv_refs[0], True)
            continue

        @pl.when(flags_ref[i] > 0)
        def _(i=i):
            update(kv_refs[i], False)

    if final:
        o_ref = outs[0]
        for g in range(KV_HEADS):
            normed = acc_sc[g] / l_sc[g]
            for j in range(grp):
                col = (g * grp + j) * HEAD_DIM
                o_ref[:, col : col + HEAD_DIM] = normed[:, j * tok : (j + 1) * tok].T
    else:
        outs[0][...] = m_sc[...]
        outs[1][...] = l_sc[...]
        outs[2][...] = acc_sc[...]


def flash(flags, query, blocks, state, final):
    tok = query.shape[0]
    grp = HEADS // KV_HEADS
    vmem = pl.BlockSpec(memory_space=pltpu.VMEM)
    stat = jax.ShapeDtypeStruct((KV_HEADS, 1, grp * tok), jnp.float32)
    acc = jax.ShapeDtypeStruct((KV_HEADS, HEAD_DIM, grp * tok), jnp.float32)
    if final:
        out_shape = jax.ShapeDtypeStruct((tok, HEADS * HEAD_DIM), jnp.float32)
        out_specs = vmem
    else:
        out_shape = (stat, stat, acc)
        out_specs = (vmem, vmem, vmem)
    first = state is None
    extra = () if first else tuple(state)
    kernel = functools.partial(flash_kernel, first, final, len(blocks))
    return pl.pallas_call(
        kernel,
        out_shape=out_shape,
        in_specs=[pl.BlockSpec(memory_space=pltpu.SMEM)]
        + [vmem] * (1 + len(extra) + len(blocks)),
        out_specs=out_specs,
        scratch_shapes=[
            pltpu.VMEM((KV_HEADS, grp * tok, HEAD_DIM), jnp.bfloat16),
            pltpu.VMEM((KV_HEADS, 1, grp * tok), jnp.float32),
            pltpu.VMEM((KV_HEADS, 1, grp * tok), jnp.float32),
            pltpu.VMEM((KV_HEADS, HEAD_DIM, grp * tok), jnp.float32),
        ],
        compiler_params=pltpu.CompilerParams(vmem_limit_bytes=48 * 1024 * 1024),
    )(flags, query, *extra, *blocks)


def attention(query, key_rows, val_rows, tok, ctx_index):
    count = lax.axis_size("ctx")
    rows = count // ROW
    kv = jnp.concatenate([key_rows, val_rows], axis=1)
    kv = kv.reshape(tok, 2 * KV_HEADS, HEAD_DIM).transpose(1, 0, 2)
    plus = [(r * ROW + z, r * ROW + (z + 1) % ROW) for r in range(rows) for z in range(ROW)]
    minus = [(r * ROW + z, r * ROW + (z - 1) % ROW) for r in range(rows) for z in range(ROW)]
    lefts, rights = [kv], [kv]
    for _ in range(ROW // 2):
        lefts.append(lax.ppermute(lefts[-1], "ctx", plus))
    for _ in range(ROW - 1 - ROW // 2):
        rights.append(lax.ppermute(rights[-1], "ctx", minus))
    row_blocks = lefts + rights[1:]
    z = ctx_index % ROW
    r = ctx_index // ROW
    flags = [jnp.int32(1)]
    flags += [(z - k >= 0).astype(jnp.int32) for k in range(1, len(lefts))]
    flags += [(z + k >= ROW).astype(jnp.int32) for k in range(1, len(rights))]
    blocks = list(row_blocks)
    for lower in range(rows - 1):
        for upper in range(lower + 1, rows):
            up = [(lower * ROW + z2, upper * ROW + z2) for z2 in range(ROW)]
            for piece in row_blocks:
                blocks.append(lax.ppermute(piece, "ctx", up))
                flags.append((r == upper).astype(jnp.int32))
    split = len(row_blocks)
    if split == len(blocks):
        return flash(jnp.stack(flags), query, blocks, None, True)
    state = flash(jnp.stack(flags[:split]), query, blocks[:split], None, False)
    return flash(jnp.stack(flags[split:]), query, blocks[split:], state, True)


def hyena_conv(first_in, value_in, filters, tok):
    width = first_in.shape[1]
    taps = filters.shape[1]
    fgroups = filters.shape[0]
    u_rows = (first_in.astype(jnp.float32) * value_in.astype(jnp.float32)).astype(jnp.bfloat16)
    before = passed_along(u_rows[tok - taps :], "ctx", 1)
    extended = jnp.concatenate([before, u_rows], 0)
    nblk = tok // taps
    blocks = extended.reshape(nblk + 1, taps, fgroups, width // fgroups)
    rows_at = jnp.arange(taps, dtype=jnp.int32)
    lag = rows_at[:, None] - rows_at[None, :]
    wrapped = (lag + taps) % taps
    selector = (wrapped[None, :, :] == rows_at[:, None, None]).astype(jnp.bfloat16)
    circulant = jnp.einsum(
        "gk,kij->gij", filters, selector, preferred_element_type=jnp.float32
    ).astype(jnp.bfloat16)
    nothing = jnp.zeros((), jnp.bfloat16)
    lower = jnp.where((lag >= 0)[None], circulant, nothing)
    upper = jnp.where((lag < 0)[None], circulant, nothing)
    conv = jnp.einsum("gij,bjgc->bigc", lower, blocks[1:], preferred_element_type=jnp.float32)
    conv = conv + jnp.einsum(
        "gij,bjgc->bigc", upper, blocks[:-1], preferred_element_type=jnp.float32
    )
    return conv.reshape(tok, width)


def blend(rows, width):
    gates = rows[:, :width].astype(jnp.float32)
    vals = rows[:, width:].astype(jnp.float32)
    return (jax.nn.sigmoid(gates) * vals).astype(jnp.bfloat16)


def place_rows(slots, rows, total_slots):
    placing = (jnp.arange(total_slots, dtype=jnp.int32)[:, None] == slots[None, :]).astype(
        jnp.bfloat16
    )
    return jnp.dot(placing, rows, preferred_element_type=jnp.float32).astype(jnp.bfloat16)


def route_hints(panels, owner, step_rows, width, tok, ctx_index):
    dp_count = lax.axis_size("dp")
    count = panels.shape[1]
    entries = panels.shape[2]
    cap = min(count, 4 * count // dp_count)
    owners = owner[0, :, 0]
    marks = (owners[:, None] == jnp.arange(dp_count, dtype=jnp.int32)[None, :]).astype(jnp.int32)
    before_mask = (
        jnp.arange(count, dtype=jnp.int32)[:, None] > jnp.arange(count, dtype=jnp.int32)[None, :]
    ).astype(jnp.int32)
    earlier = jnp.sum(jnp.dot(before_mask, marks) * marks, axis=1)
    slots = owners * cap + earlier
    base_row = ctx_index * tok
    row_buffer = jnp.full((dp_count * cap,), base_row, jnp.int32).at[slots].set(step_rows[0])
    arrived_rows = (
        lax.all_to_all(
            row_buffer.reshape(dp_count, cap), "dp", split_axis=0, concat_axis=0, tiled=True
        ).reshape(dp_count * cap)
        - base_row
    )
    buffer = place_rows(slots, panels[0], dp_count * cap)
    received = lax.all_to_all(
        buffer.reshape(dp_count, cap, entries), "dp", split_axis=0, concat_axis=0, tiled=True
    )
    arrived = blend(received.reshape(dp_count * cap, entries), width)
    landing = (jnp.arange(tok, dtype=jnp.int32)[:, None] == arrived_rows[None, :]).astype(
        jnp.bfloat16
    )
    return jnp.dot(landing, arrived, preferred_element_type=jnp.float32)


def per_device(
    queries, keys, values, hyena_x1, hyena_x2, hyena_v, filters, panels, owner, step_rows
):
    tok = queries.shape[1]
    width = hyena_x1.shape[2]
    ctx_index = lax.axis_index("ctx")
    conv = hyena_conv(hyena_x1[0], hyena_v[0], filters, tok)
    attended = attention(queries[0], keys[0], values[0], tok, ctx_index)
    hints = route_hints(panels, owner, step_rows, width, tok, ctx_index)
    total = hyena_x2[0].astype(jnp.float32) * conv + attended + hints
    return total.astype(jnp.bfloat16)[None]


def solution(mesh):
    placed = (
        P("dp", "ctx", None),
        P("dp", "ctx", None),
        P("dp", "ctx", None),
        P("dp", "ctx", None),
        P("dp", "ctx", None),
        P("dp", "ctx", None),
        P(),
        P("dp", "ctx", None),
        P("dp", "ctx", None),
        P("dp", "ctx"),
    )
    return jax.shard_map(
        per_device, mesh=mesh, in_specs=placed, out_specs=P("dp", "ctx", None), check_vma=False
    )
```

```python
import functools

import jax
import jax.numpy as jnp
from jax import lax
from jax.sharding import PartitionSpec as P
from jax.experimental import pallas as pl
from jax.experimental.pallas import tpu as pltpu

HEADS = 16
KV_HEADS = 4
HEAD_DIM = 128


NEG = -1e30


def passed_along(block, axis, distance):
    devices = range(lax.axis_size(axis))
    route = [(i - distance, i) for i in devices if i - distance in devices]
    return lax.ppermute(block, axis, route)


ROW = 8


def flash_kernel(first, final, count, *refs):
    flags_ref, q_ref = refs[0], refs[1]
    at = 2
    if not first:
        m_in, l_in, acc_in = refs[at : at + 3]
        at += 3
    kv_refs = refs[at : at + count]
    at += count
    outs = refs[at : at + (1 if final else 3)]
    qs_sc, m_sc, l_sc, acc_sc = refs[at + len(outs) :]
    grp = HEADS // KV_HEADS
    tok = q_ref.shape[0]
    scale = HEAD_DIM ** (-0.5)

    for g in range(KV_HEADS):
        for j in range(grp):
            col = (g * grp + j) * HEAD_DIM
            qs_sc[g, j * tok : (j + 1) * tok, :] = q_ref[:, col : col + HEAD_DIM]
    if first:
        m_sc[...] = jnp.full_like(m_sc, NEG)
        l_sc[...] = jnp.zeros_like(l_sc)
        acc_sc[...] = jnp.zeros_like(acc_sc)
    else:
        m_sc[...] = m_in[...]
        l_sc[...] = l_in[...]
        acc_sc[...] = acc_in[...]

    def update(kv_ref, masked):
        def one(g, carry):
            k = kv_ref[g]
            v = kv_ref[KV_HEADS + g]
            s = lax.dot_general(
                k, qs_sc[g], (((1,), (1,)), ((), ())), preferred_element_type=jnp.float32
            ) * scale
            if masked:
                rows = lax.broadcasted_iota(jnp.int32, s.shape, 0)
                cols = lax.broadcasted_iota(jnp.int32, s.shape, 1) % tok
                s = jnp.where(rows <= cols, s, NEG)
            m_old = m_sc[g]
            m_new = jnp.maximum(m_old, jnp.max(s, axis=0, keepdims=True))
            p = jnp.exp(s - m_new)
            alpha = jnp.exp(m_old - m_new)
            l_sc[g] = alpha * l_sc[g] + jnp.sum(p, axis=0, keepdims=True)
            pv = lax.dot_general(
                v, p.astype(jnp.bfloat16), (((0,), (0,)), ((), ())),
                preferred_element_type=jnp.float32,
            )
            acc_sc[g] = alpha * acc_sc[g] + pv
            m_sc[g] = m_new
            return carry

        lax.fori_loop(0, KV_HEADS, one, 0)

    for i in range(count):
        if first and i == 0:
            update(kv_refs[0], True)
            continue

        @pl.when(flags_ref[i] > 0)
        def _(i=i):
            update(kv_refs[i], False)

    if final:
        o_ref = outs[0]
        for g in range(KV_HEADS):
            normed = acc_sc[g] / l_sc[g]
            for j in range(grp):
                col = (g * grp + j) * HEAD_DIM
                o_ref[:, col : col + HEAD_DIM] = normed[:, j * tok : (j + 1) * tok].T
    else:
        outs[0][...] = m_sc[...]
        outs[1][...] = l_sc[...]
        outs[2][...] = acc_sc[...]


def flash(flags, query, blocks, state, final):
    tok = query.shape[0]
    grp = HEADS // KV_HEADS
    vmem = pl.BlockSpec(memory_space=pltpu.VMEM)
    stat = jax.ShapeDtypeStruct((KV_HEADS, 1, grp * tok), jnp.float32)
    acc = jax.ShapeDtypeStruct((KV_HEADS, HEAD_DIM, grp * tok), jnp.float32)
    if final:
        out_shape = jax.ShapeDtypeStruct((tok, HEADS * HEAD_DIM), jnp.float32)
        out_specs = vmem
    else:
        out_shape = (stat, stat, acc)
        out_specs = (vmem, vmem, vmem)
    first = state is None
    extra = () if first else tuple(state)
    kernel = functools.partial(flash_kernel, first, final, len(blocks))
    return pl.pallas_call(
        kernel,
        out_shape=out_shape,
        in_specs=[pl.BlockSpec(memory_space=pltpu.SMEM)]
        + [vmem] * (1 + len(extra) + len(blocks)),
        out_specs=out_specs,
        scratch_shapes=[
            pltpu.VMEM((KV_HEADS, grp * tok, HEAD_DIM), jnp.bfloat16),
            pltpu.VMEM((KV_HEADS, 1, grp * tok), jnp.float32),
            pltpu.VMEM((KV_HEADS, 1, grp * tok), jnp.float32),
            pltpu.VMEM((KV_HEADS, HEAD_DIM, grp * tok), jnp.float32),
        ],
        compiler_params=pltpu.CompilerParams(vmem_limit_bytes=48 * 1024 * 1024),
    )(flags, query, *extra, *blocks)


def attention(query, key_rows, val_rows, tok, ctx_index):
    count = lax.axis_size("ctx")
    rows = count // ROW
    kv = jnp.concatenate([key_rows, val_rows], axis=1)
    kv = kv.reshape(tok, 2 * KV_HEADS, HEAD_DIM).transpose(1, 0, 2)
    plus = [(r * ROW + z, r * ROW + (z + 1) % ROW) for r in range(rows) for z in range(ROW)]
    minus = [(r * ROW + z, r * ROW + (z - 1) % ROW) for r in range(rows) for z in range(ROW)]
    lefts, rights = [kv], [kv]
    for _ in range(ROW // 2):
        lefts.append(lax.ppermute(lefts[-1], "ctx", plus))
    for _ in range(ROW - 1 - ROW // 2):
        rights.append(lax.ppermute(rights[-1], "ctx", minus))
    row_blocks = [kv]
    for k in range(1, max(len(lefts), len(rights))):
        row_blocks += [side[k] for side in (lefts, rights) if k < len(side)]
    z = ctx_index % ROW
    r = ctx_index // ROW
    flags = [jnp.int32(1)]
    for k in range(1, max(len(lefts), len(rights))):
        if k < len(lefts):
            flags.append((z - k >= 0).astype(jnp.int32))
        if k < len(rights):
            flags.append((z + k >= ROW).astype(jnp.int32))
    blocks = list(row_blocks)
    for lower in range(rows - 1):
        for upper in range(lower + 1, rows):
            up = [(lower * ROW + z2, upper * ROW + z2) for z2 in range(ROW)]
            for piece in row_blocks:
                blocks.append(lax.ppermute(piece, "ctx", up))
                flags.append((r == upper).astype(jnp.int32))
    split = len(row_blocks)
    if split == len(blocks):
        return flash(jnp.stack(flags), query, blocks, None, True)
    state = flash(jnp.stack(flags[:split]), query, blocks[:split], None, False)
    late = split + len(row_blocks) - 3
    state = flash(jnp.stack(flags[split:late]), query, blocks[split:late], state, False)
    return flash(jnp.stack(flags[late:]), query, blocks[late:], state, True)


def hyena_conv(first_in, value_in, filters, tok):
    width = first_in.shape[1]
    taps = filters.shape[1]
    fgroups = filters.shape[0]
    u_rows = (first_in.astype(jnp.float32) * value_in.astype(jnp.float32)).astype(jnp.bfloat16)
    before = passed_along(u_rows[tok - taps :], "ctx", 1)
    return conv_body(before, u_rows, filters, tok, width, taps, fgroups)


def conv_body(before, u_rows, filters, tok, width, taps, fgroups):
    extended = jnp.concatenate([before, u_rows], 0)
    nblk = tok // taps
    blocks = extended.reshape(nblk + 1, taps, fgroups, width // fgroups)
    rows_at = jnp.arange(taps, dtype=jnp.int32)
    lag = rows_at[:, None] - rows_at[None, :]
    wrapped = (lag + taps) % taps
    selector = (wrapped[None, :, :] == rows_at[:, None, None]).astype(jnp.bfloat16)
    circulant = jnp.einsum(
        "gk,kij->gij", filters, selector, preferred_element_type=jnp.float32
    ).astype(jnp.bfloat16)
    nothing = jnp.zeros((), jnp.bfloat16)
    lower = jnp.where((lag >= 0)[None], circulant, nothing)
    upper = jnp.where((lag < 0)[None], circulant, nothing)
    conv = jnp.einsum("gij,bjgc->bigc", lower, blocks[1:], preferred_element_type=jnp.float32)
    conv = conv + jnp.einsum(
        "gij,bjgc->bigc", upper, blocks[:-1], preferred_element_type=jnp.float32
    )
    return conv.reshape(tok, width)


def blend(rows, width):
    gates = rows[:, :width].astype(jnp.float32)
    vals = rows[:, width:].astype(jnp.float32)
    return (jax.nn.sigmoid(gates) * vals).astype(jnp.bfloat16)


def place_rows(slots, rows, total_slots):
    placing = (jnp.arange(total_slots, dtype=jnp.int32)[:, None] == slots[None, :]).astype(
        jnp.bfloat16
    )
    return jnp.dot(placing, rows, preferred_element_type=jnp.float32).astype(jnp.bfloat16)


def route_hints(panels, owner, step_rows, width, tok, ctx_index):
    dp_count = lax.axis_size("dp")
    count = panels.shape[1]
    entries = panels.shape[2]
    cap = min(count, 4 * count // dp_count)
    owners = owner[0, :, 0]
    marks = (owners[:, None] == jnp.arange(dp_count, dtype=jnp.int32)[None, :]).astype(jnp.int32)
    before_mask = (
        jnp.arange(count, dtype=jnp.int32)[:, None] > jnp.arange(count, dtype=jnp.int32)[None, :]
    ).astype(jnp.int32)
    earlier = jnp.sum(jnp.dot(before_mask, marks) * marks, axis=1)
    slots = owners * cap + earlier
    base_row = ctx_index * tok
    row_buffer = jnp.full((dp_count * cap,), base_row, jnp.int32).at[slots].set(step_rows[0])
    arrived_rows = (
        lax.all_to_all(
            row_buffer.reshape(dp_count, cap), "dp", split_axis=0, concat_axis=0, tiled=True
        ).reshape(dp_count * cap)
        - base_row
    )
    buffer = place_rows(slots, panels[0], dp_count * cap)
    received = lax.all_to_all(
        buffer.reshape(dp_count, cap, entries), "dp", split_axis=0, concat_axis=0, tiled=True
    )
    arrived = blend(received.reshape(dp_count * cap, entries), width)
    landing = (jnp.arange(tok, dtype=jnp.int32)[:, None] == arrived_rows[None, :]).astype(
        jnp.bfloat16
    )
    return jnp.dot(landing, arrived, preferred_element_type=jnp.float32)


def per_device(
    queries, keys, values, hyena_x1, hyena_x2, hyena_v, filters, panels, owner, step_rows
):
    tok = queries.shape[1]
    width = hyena_x1.shape[2]
    ctx_index = lax.axis_index("ctx")
    conv = hyena_conv(hyena_x1[0], hyena_v[0], filters, tok)
    attended = attention(queries[0], keys[0], values[0], tok, ctx_index)
    hints = route_hints(panels, owner, step_rows, width, tok, ctx_index)
    total = hyena_x2[0].astype(jnp.float32) * conv + attended + hints
    return total.astype(jnp.bfloat16)[None]


def solution(mesh):
    placed = (
        P("dp", "ctx", None),
        P("dp", "ctx", None),
        P("dp", "ctx", None),
        P("dp", "ctx", None),
        P("dp", "ctx", None),
        P("dp", "ctx", None),
        P(),
        P("dp", "ctx", None),
        P("dp", "ctx", None),
        P("dp", "ctx"),
    )
    return jax.shard_map(
        per_device, mesh=mesh, in_specs=placed, out_specs=P("dp", "ctx", None), check_vma=False
    )
```

```python
import functools

import jax
import jax.numpy as jnp
from jax import lax
from jax.sharding import PartitionSpec as P
from jax.experimental import pallas as pl
from jax.experimental.pallas import tpu as pltpu

HEADS = 16
KV_HEADS = 4
HEAD_DIM = 128


NEG = -1e30


def passed_along(block, axis, distance):
    devices = range(lax.axis_size(axis))
    route = [(i - distance, i) for i in devices if i - distance in devices]
    return lax.ppermute(block, axis, route)


ROW = 8


def flash_kernel(first, final, count, *refs):
    flags_ref, q_ref = refs[0], refs[1]
    at = 2
    if not first:
        m_in, l_in, acc_in = refs[at : at + 3]
        at += 3
    kv_refs = refs[at : at + count]
    at += count
    outs = refs[at : at + (1 if final else 3)]
    qs_sc, m_sc, l_sc, acc_sc = refs[at + len(outs) :]
    grp = HEADS // KV_HEADS
    tok = q_ref.shape[0]
    scale = HEAD_DIM ** (-0.5)

    for g in range(KV_HEADS):
        for j in range(grp):
            col = (g * grp + j) * HEAD_DIM
            qs_sc[g, :, j * tok : (j + 1) * tok] = q_ref[:, col : col + HEAD_DIM].T
    if first:
        m_sc[...] = jnp.full_like(m_sc, NEG)
        l_sc[...] = jnp.zeros_like(l_sc)
        acc_sc[...] = jnp.zeros_like(acc_sc)
    else:
        m_sc[...] = m_in[...]
        l_sc[...] = l_in[...]
        acc_sc[...] = acc_in[...]

    def update(kv_ref, masked):
        def one(g, carry):
            k = kv_ref[g]
            v = kv_ref[KV_HEADS + g]
            s = jnp.dot(k, qs_sc[g], preferred_element_type=jnp.float32) * scale
            if masked:
                rows = lax.broadcasted_iota(jnp.int32, s.shape, 0)
                cols = lax.broadcasted_iota(jnp.int32, s.shape, 1) % tok
                s = jnp.where(rows <= cols, s, NEG)
            m_old = m_sc[g]
            m_new = jnp.maximum(m_old, jnp.max(s, axis=0, keepdims=True))
            p = jnp.exp(s - m_new)
            alpha = jnp.exp(m_old - m_new)
            l_sc[g] = alpha * l_sc[g] + jnp.sum(p, axis=0, keepdims=True)
            pv = lax.dot_general(
                v, p.astype(jnp.bfloat16), (((0,), (0,)), ((), ())),
                preferred_element_type=jnp.float32,
            )
            acc_sc[g] = alpha * acc_sc[g] + pv
            m_sc[g] = m_new
            return carry

        lax.fori_loop(0, KV_HEADS, one, 0)

    for i in range(count):
        if first and i == 0:
            update(kv_refs[0], True)
            continue

        @pl.when(flags_ref[i] > 0)
        def _(i=i):
            update(kv_refs[i], False)

    if final:
        o_ref = outs[0]
        for g in range(KV_HEADS):
            normed = acc_sc[g] / l_sc[g]
            for j in range(grp):
                col = (g * grp + j) * HEAD_DIM
                o_ref[:, col : col + HEAD_DIM] = normed[:, j * tok : (j + 1) * tok].T
    else:
        outs[0][...] = m_sc[...]
        outs[1][...] = l_sc[...]
        outs[2][...] = acc_sc[...]


def flash(flags, query, blocks, state, final):
    tok = query.shape[0]
    grp = HEADS // KV_HEADS
    vmem = pl.BlockSpec(memory_space=pltpu.VMEM)
    stat = jax.ShapeDtypeStruct((KV_HEADS, 1, grp * tok), jnp.float32)
    acc = jax.ShapeDtypeStruct((KV_HEADS, HEAD_DIM, grp * tok), jnp.float32)
    if final:
        out_shape = jax.ShapeDtypeStruct((tok, HEADS * HEAD_DIM), jnp.float32)
        out_specs = vmem
    else:
        out_shape = (stat, stat, acc)
        out_specs = (vmem, vmem, vmem)
    first = state is None
    extra = () if first else tuple(state)
    kernel = functools.partial(flash_kernel, first, final, len(blocks))
    return pl.pallas_call(
        kernel,
        out_shape=out_shape,
        in_specs=[pl.BlockSpec(memory_space=pltpu.SMEM)]
        + [vmem] * (1 + len(extra) + len(blocks)),
        out_specs=out_specs,
        scratch_shapes=[
            pltpu.VMEM((KV_HEADS, HEAD_DIM, grp * tok), jnp.bfloat16),
            pltpu.VMEM((KV_HEADS, 1, grp * tok), jnp.float32),
            pltpu.VMEM((KV_HEADS, 1, grp * tok), jnp.float32),
            pltpu.VMEM((KV_HEADS, HEAD_DIM, grp * tok), jnp.float32),
        ],
        compiler_params=pltpu.CompilerParams(vmem_limit_bytes=48 * 1024 * 1024),
    )(flags, query, *extra, *blocks)


def attention(query, key_rows, val_rows, tok, ctx_index):
    count = lax.axis_size("ctx")
    rows = count // ROW
    kv = jnp.concatenate([key_rows, val_rows], axis=1)
    kv = kv.reshape(tok, 2 * KV_HEADS, HEAD_DIM).transpose(1, 0, 2)
    plus = [(r * ROW + z, r * ROW + (z + 1) % ROW) for r in range(rows) for z in range(ROW)]
    minus = [(r * ROW + z, r * ROW + (z - 1) % ROW) for r in range(rows) for z in range(ROW)]
    lefts, rights = [kv], [kv]
    for _ in range(ROW // 2):
        lefts.append(lax.ppermute(lefts[-1], "ctx", plus))
    for _ in range(ROW - 1 - ROW // 2):
        rights.append(lax.ppermute(rights[-1], "ctx", minus))
    row_blocks = [kv]
    for k in range(1, max(len(lefts), len(rights))):
        row_blocks += [side[k] for side in (lefts, rights) if k < len(side)]
    z = ctx_index % ROW
    r = ctx_index // ROW
    flags = [jnp.int32(1)]
    for k in range(1, max(len(lefts), len(rights))):
        if k < len(lefts):
            flags.append((z - k >= 0).astype(jnp.int32))
        if k < len(rights):
            flags.append((z + k >= ROW).astype(jnp.int32))
    blocks = list(row_blocks)
    for lower in range(rows - 1):
        for upper in range(lower + 1, rows):
            up = [(lower * ROW + z2, upper * ROW + z2) for z2 in range(ROW)]
            for piece in row_blocks:
                blocks.append(lax.ppermute(piece, "ctx", up))
                flags.append((r == upper).astype(jnp.int32))
    split = len(row_blocks)
    if split == len(blocks):
        return flash(jnp.stack(flags), query, blocks, None, True)
    state = flash(jnp.stack(flags[:split]), query, blocks[:split], None, False)
    late = split + len(row_blocks) - 3
    state = flash(jnp.stack(flags[split:late]), query, blocks[split:late], state, False)
    return flash(jnp.stack(flags[late:]), query, blocks[late:], state, True)


def hyena_conv(first_in, value_in, filters, tok):
    width = first_in.shape[1]
    taps = filters.shape[1]
    fgroups = filters.shape[0]
    u_rows = (first_in.astype(jnp.float32) * value_in.astype(jnp.float32)).astype(jnp.bfloat16)
    before = passed_along(u_rows[tok - taps :], "ctx", 1)
    return conv_body(before, u_rows, filters, tok, width, taps, fgroups)


def conv_body(before, u_rows, filters, tok, width, taps, fgroups):
    extended = jnp.concatenate([before, u_rows], 0)
    nblk = tok // taps
    blocks = extended.reshape(nblk + 1, taps, fgroups, width // fgroups)
    rows_at = jnp.arange(taps, dtype=jnp.int32)
    lag = rows_at[:, None] - rows_at[None, :]
    wrapped = (lag + taps) % taps
    selector = (wrapped[None, :, :] == rows_at[:, None, None]).astype(jnp.bfloat16)
    circulant = jnp.einsum(
        "gk,kij->gij", filters, selector, preferred_element_type=jnp.float32
    ).astype(jnp.bfloat16)
    nothing = jnp.zeros((), jnp.bfloat16)
    lower = jnp.where((lag >= 0)[None], circulant, nothing)
    upper = jnp.where((lag < 0)[None], circulant, nothing)
    conv = jnp.einsum("gij,bjgc->bigc", lower, blocks[1:], preferred_element_type=jnp.float32)
    conv = conv + jnp.einsum(
        "gij,bjgc->bigc", upper, blocks[:-1], preferred_element_type=jnp.float32
    )
    return conv.reshape(tok, width)


def blend(rows, width):
    gates = rows[:, :width].astype(jnp.float32)
    vals = rows[:, width:].astype(jnp.float32)
    return (jax.nn.sigmoid(gates) * vals).astype(jnp.bfloat16)


def place_rows(slots, rows, total_slots):
    placing = (jnp.arange(total_slots, dtype=jnp.int32)[:, None] == slots[None, :]).astype(
        jnp.bfloat16
    )
    return jnp.dot(placing, rows, preferred_element_type=jnp.float32).astype(jnp.bfloat16)


def route_hints(panels, owner, step_rows, width, tok, ctx_index):
    dp_count = lax.axis_size("dp")
    count = panels.shape[1]
    entries = panels.shape[2]
    cap = min(count, 4 * count // dp_count)
    owners = owner[0, :, 0]
    marks = (owners[:, None] == jnp.arange(dp_count, dtype=jnp.int32)[None, :]).astype(jnp.int32)
    before_mask = (
        jnp.arange(count, dtype=jnp.int32)[:, None] > jnp.arange(count, dtype=jnp.int32)[None, :]
    ).astype(jnp.int32)
    earlier = jnp.sum(jnp.dot(before_mask, marks) * marks, axis=1)
    slots = owners * cap + earlier
    base_row = ctx_index * tok
    row_buffer = jnp.full((dp_count * cap,), base_row, jnp.int32).at[slots].set(step_rows[0])
    arrived_rows = (
        lax.all_to_all(
            row_buffer.reshape(dp_count, cap), "dp", split_axis=0, concat_axis=0, tiled=True
        ).reshape(dp_count * cap)
        - base_row
    )
    buffer = place_rows(slots, panels[0], dp_count * cap)
    received = lax.all_to_all(
        buffer.reshape(dp_count, cap, entries), "dp", split_axis=0, concat_axis=0, tiled=True
    )
    arrived = blend(received.reshape(dp_count * cap, entries), width)
    landing = (jnp.arange(tok, dtype=jnp.int32)[:, None] == arrived_rows[None, :]).astype(
        jnp.bfloat16
    )
    return jnp.dot(landing, arrived, preferred_element_type=jnp.float32)


def per_device(
    queries, keys, values, hyena_x1, hyena_x2, hyena_v, filters, panels, owner, step_rows
):
    tok = queries.shape[1]
    width = hyena_x1.shape[2]
    ctx_index = lax.axis_index("ctx")
    conv = hyena_conv(hyena_x1[0], hyena_v[0], filters, tok)
    attended = attention(queries[0], keys[0], values[0], tok, ctx_index)
    hints = route_hints(panels, owner, step_rows, width, tok, ctx_index)
    total = hyena_x2[0].astype(jnp.float32) * conv + attended + hints
    return total.astype(jnp.bfloat16)[None]


def solution(mesh):
    placed = (
        P("dp", "ctx", None),
        P("dp", "ctx", None),
        P("dp", "ctx", None),
        P("dp", "ctx", None),
        P("dp", "ctx", None),
        P("dp", "ctx", None),
        P(),
        P("dp", "ctx", None),
        P("dp", "ctx", None),
        P("dp", "ctx"),
    )
    return jax.shard_map(
        per_device, mesh=mesh, in_specs=placed, out_specs=P("dp", "ctx", None), check_vma=False
    )
```

```python
import functools

import jax
import jax.numpy as jnp
from jax import lax
from jax.sharding import PartitionSpec as P
from jax.experimental import pallas as pl
from jax.experimental.pallas import tpu as pltpu

HEADS = 16
KV_HEADS = 4
HEAD_DIM = 128


NEG = -1e30


def passed_along(block, axis, distance):
    devices = range(lax.axis_size(axis))
    route = [(i - distance, i) for i in devices if i - distance in devices]
    return lax.ppermute(block, axis, route)


ROW = 8


def flash_kernel(first, final, count, *refs):
    flags_ref, q_ref = refs[0], refs[1]
    at = 2
    if not first:
        m_in, l_in, acc_in = refs[at : at + 3]
        at += 3
    kv_refs = refs[at : at + count]
    at += count
    outs = refs[at : at + (1 if final else 3)]
    qs_sc, m_sc, l_sc, acc_sc = refs[at + len(outs) :]
    grp = HEADS // KV_HEADS
    tok = q_ref.shape[0]
    scale = HEAD_DIM ** (-0.5)

    for g in range(KV_HEADS):
        for j in range(grp):
            col = (g * grp + j) * HEAD_DIM
            qs_sc[g, :, j * tok : (j + 1) * tok] = q_ref[:, col : col + HEAD_DIM].T
    if first:
        m_sc[...] = jnp.full_like(m_sc, NEG)
        l_sc[...] = jnp.zeros_like(l_sc)
        acc_sc[...] = jnp.zeros_like(acc_sc)
    else:
        m_sc[...] = m_in[...]
        l_sc[...] = l_in[...]
        acc_sc[...] = acc_in[...]

    def update(kv_ref, masked):
        def one(g, carry):
            k = kv_ref[g]
            v = kv_ref[KV_HEADS + g]
            s = jnp.dot(k, qs_sc[g], preferred_element_type=jnp.float32) * scale
            if masked:
                rows = lax.broadcasted_iota(jnp.int32, s.shape, 0)
                cols = lax.broadcasted_iota(jnp.int32, s.shape, 1) % tok
                s = jnp.where(rows <= cols, s, NEG)
            m_old = m_sc[g]
            m_new = jnp.maximum(m_old, jnp.max(s, axis=0, keepdims=True))
            p = jnp.exp(s - m_new)
            alpha = jnp.exp(m_old - m_new)
            l_sc[g] = alpha * l_sc[g] + jnp.sum(p, axis=0, keepdims=True)
            pv = lax.dot_general(
                v, p.astype(jnp.bfloat16), (((0,), (0,)), ((), ())),
                preferred_element_type=jnp.float32,
            )
            acc_sc[g] = alpha * acc_sc[g] + pv
            m_sc[g] = m_new
            return carry

        lax.fori_loop(0, KV_HEADS, one, 0)

    for i in range(count):
        if first and i == 0:
            update(kv_refs[0], True)
            continue

        @pl.when(flags_ref[i] > 0)
        def _(i=i):
            update(kv_refs[i], False)

    if final:
        o_ref = outs[0]
        for g in range(KV_HEADS):
            normed = acc_sc[g] / l_sc[g]
            for j in range(grp):
                col = (g * grp + j) * HEAD_DIM
                o_ref[:, col : col + HEAD_DIM] = normed[:, j * tok : (j + 1) * tok].T
    else:
        outs[0][...] = m_sc[...]
        outs[1][...] = l_sc[...]
        outs[2][...] = acc_sc[...]


def flash(flags, query, blocks, state, final):
    tok = query.shape[0]
    grp = HEADS // KV_HEADS
    vmem = pl.BlockSpec(memory_space=pltpu.VMEM)
    stat = jax.ShapeDtypeStruct((KV_HEADS, 1, grp * tok), jnp.float32)
    acc = jax.ShapeDtypeStruct((KV_HEADS, HEAD_DIM, grp * tok), jnp.float32)
    if final:
        out_shape = jax.ShapeDtypeStruct((tok, HEADS * HEAD_DIM), jnp.float32)
        out_specs = vmem
    else:
        out_shape = (stat, stat, acc)
        out_specs = (vmem, vmem, vmem)
    first = state is None
    extra = () if first else tuple(state)
    kernel = functools.partial(flash_kernel, first, final, len(blocks))
    return pl.pallas_call(
        kernel,
        out_shape=out_shape,
        in_specs=[pl.BlockSpec(memory_space=pltpu.SMEM)]
        + [vmem] * (1 + len(extra) + len(blocks)),
        out_specs=out_specs,
        scratch_shapes=[
            pltpu.VMEM((KV_HEADS, HEAD_DIM, grp * tok), jnp.bfloat16),
            pltpu.VMEM((KV_HEADS, 1, grp * tok), jnp.float32),
            pltpu.VMEM((KV_HEADS, 1, grp * tok), jnp.float32),
            pltpu.VMEM((KV_HEADS, HEAD_DIM, grp * tok), jnp.float32),
        ],
        compiler_params=pltpu.CompilerParams(vmem_limit_bytes=48 * 1024 * 1024),
    )(flags, query, *extra, *blocks)


def attention(query, key_rows, val_rows, tok, ctx_index):
    count = lax.axis_size("ctx")
    rows = count // ROW
    kv = jnp.concatenate([key_rows, val_rows], axis=1)
    kv = kv.reshape(tok, 2 * KV_HEADS, HEAD_DIM).transpose(1, 0, 2)
    plus = [(r * ROW + z, r * ROW + (z + 1) % ROW) for r in range(rows) for z in range(ROW)]
    minus = [(r * ROW + z, r * ROW + (z - 1) % ROW) for r in range(rows) for z in range(ROW)]
    lefts, rights = [kv], [kv]
    lefts.append(lax.ppermute(kv, "ctx", plus))
    rights.append(lax.ppermute(kv, "ctx", minus))
    for _ in range(ROW // 2 - 1):
        lefts.append(lax.ppermute(lefts[-1], "ctx", plus))
    for _ in range(ROW - 2 - ROW // 2):
        rights.append(lax.ppermute(rights[-1], "ctx", minus))
    row_blocks = [kv]
    for k in range(1, max(len(lefts), len(rights))):
        row_blocks += [side[k] for side in (lefts, rights) if k < len(side)]
    z = ctx_index % ROW
    r = ctx_index // ROW
    flags = [jnp.int32(1)]
    for k in range(1, max(len(lefts), len(rights))):
        if k < len(lefts):
            flags.append((z - k >= 0).astype(jnp.int32))
        if k < len(rights):
            flags.append((z + k >= ROW).astype(jnp.int32))
    blocks = list(row_blocks)
    for lower in range(rows - 1):
        for upper in range(lower + 1, rows):
            up = [(lower * ROW + z2, upper * ROW + z2) for z2 in range(ROW)]
            for piece in row_blocks:
                blocks.append(lax.ppermute(piece, "ctx", up))
                flags.append((r == upper).astype(jnp.int32))
    split = len(row_blocks)
    if split == len(blocks):
        return flash(jnp.stack(flags), query, blocks, None, True)
    state = flash(jnp.stack(flags[:split]), query, blocks[:split], None, False)
    late = split + len(row_blocks) - 3
    last = len(blocks) - 1
    state = flash(jnp.stack(flags[split:late]), query, blocks[split:late], state, False)
    state = flash(jnp.stack(flags[late:last]), query, blocks[late:last], state, False)
    return flash(jnp.stack(flags[last:]), query, blocks[last:], state, True)


def hyena_conv(first_in, value_in, filters, tok):
    width = first_in.shape[1]
    taps = filters.shape[1]
    fgroups = filters.shape[0]
    lower, upper = circulant_parts(filters, taps)
    u_rows = (first_in.astype(jnp.float32) * value_in.astype(jnp.float32)).astype(jnp.bfloat16)
    before = passed_along(u_rows[tok - taps :], "ctx", 1)
    return conv_body(before, u_rows, lower, upper, tok, width, taps, fgroups)


def circulant_parts(filters, taps):
    rows_at = jnp.arange(taps, dtype=jnp.int32)
    lag = rows_at[:, None] - rows_at[None, :]
    wrapped = (lag + taps) % taps
    selector = (wrapped[None, :, :] == rows_at[:, None, None]).astype(jnp.bfloat16)
    circulant = jnp.einsum(
        "gk,kij->gij", filters, selector, preferred_element_type=jnp.float32
    ).astype(jnp.bfloat16)
    nothing = jnp.zeros((), jnp.bfloat16)
    lower = jnp.where((lag >= 0)[None], circulant, nothing)
    upper = jnp.where((lag < 0)[None], circulant, nothing)
    return lower, upper


def conv_body(before, u_rows, lower, upper, tok, width, taps, fgroups):
    extended = jnp.concatenate([before, u_rows], 0)
    nblk = tok // taps
    blocks = extended.reshape(nblk + 1, taps, fgroups, width // fgroups)
    conv = jnp.einsum("gij,bjgc->bigc", lower, blocks[1:], preferred_element_type=jnp.float32)
    conv = conv + jnp.einsum(
        "gij,bjgc->bigc", upper, blocks[:-1], preferred_element_type=jnp.float32
    )
    return conv.reshape(tok, width)


def blend(rows, width):
    gates = rows[:, :width].astype(jnp.float32)
    vals = rows[:, width:].astype(jnp.float32)
    return (jax.nn.sigmoid(gates) * vals).astype(jnp.bfloat16)


def place_rows(slots, rows, total_slots):
    placing = (jnp.arange(total_slots, dtype=jnp.int32)[:, None] == slots[None, :]).astype(
        jnp.bfloat16
    )
    return jnp.dot(placing, rows, preferred_element_type=jnp.float32).astype(jnp.bfloat16)


def route_hints(panels, owner, step_rows, width, tok, ctx_index):
    dp_count = lax.axis_size("dp")
    count = panels.shape[1]
    entries = panels.shape[2]
    cap = min(count, 4 * count // dp_count)
    owners = owner[0, :, 0]
    marks = (owners[:, None] == jnp.arange(dp_count, dtype=jnp.int32)[None, :]).astype(jnp.int32)
    before_mask = (
        jnp.arange(count, dtype=jnp.int32)[:, None] > jnp.arange(count, dtype=jnp.int32)[None, :]
    ).astype(jnp.int32)
    earlier = jnp.sum(jnp.dot(before_mask, marks) * marks, axis=1)
    slots = owners * cap + earlier
    base_row = ctx_index * tok
    row_buffer = jnp.full((dp_count * cap,), base_row, jnp.int32).at[slots].set(step_rows[0])
    arrived_rows = (
        lax.all_to_all(
            row_buffer.reshape(dp_count, cap), "dp", split_axis=0, concat_axis=0, tiled=True
        ).reshape(dp_count * cap)
        - base_row
    )
    buffer = place_rows(slots, panels[0], dp_count * cap)
    received = lax.all_to_all(
        buffer.reshape(dp_count, cap, entries), "dp", split_axis=0, concat_axis=0, tiled=True
    )
    arrived = blend(received.reshape(dp_count * cap, entries), width)
    landing = (jnp.arange(tok, dtype=jnp.int32)[:, None] == arrived_rows[None, :]).astype(
        jnp.bfloat16
    )
    return jnp.dot(landing, arrived, preferred_element_type=jnp.float32)


def per_device(
    queries, keys, values, hyena_x1, hyena_x2, hyena_v, filters, panels, owner, step_rows
):
    tok = queries.shape[1]
    width = hyena_x1.shape[2]
    ctx_index = lax.axis_index("ctx")
    conv = hyena_conv(hyena_x1[0], hyena_v[0], filters, tok)
    attended = attention(queries[0], keys[0], values[0], tok, ctx_index)
    hints = route_hints(panels, owner, step_rows, width, tok, ctx_index)
    total = hyena_x2[0].astype(jnp.float32) * conv + attended + hints
    return total.astype(jnp.bfloat16)[None]


def solution(mesh):
    placed = (
        P("dp", "ctx", None),
        P("dp", "ctx", None),
        P("dp", "ctx", None),
        P("dp", "ctx", None),
        P("dp", "ctx", None),
        P("dp", "ctx", None),
        P(),
        P("dp", "ctx", None),
        P("dp", "ctx", None),
        P("dp", "ctx"),
    )
    return jax.shard_map(
        per_device, mesh=mesh, in_specs=placed, out_specs=P("dp", "ctx", None), check_vma=False
    )
```

```python
import functools

import jax
import jax.numpy as jnp
from jax import lax
from jax.sharding import PartitionSpec as P
from jax.experimental import pallas as pl
from jax.experimental.pallas import tpu as pltpu

HEADS = 16
KV_HEADS = 4
HEAD_DIM = 128


NEG = -1e30


def passed_along(block, axis, distance):
    devices = range(lax.axis_size(axis))
    route = [(i - distance, i) for i in devices if i - distance in devices]
    return lax.ppermute(block, axis, route)


ROW = 8


def flash_kernel(first, final, count, *refs):
    flags_ref, q_ref = refs[0], refs[1]
    at = 2
    if not first:
        m_in, l_in, acc_in = refs[at : at + 3]
        at += 3
    kv_refs = refs[at : at + count]
    at += count
    outs = refs[at : at + (1 if final else 3)]
    qs_sc, m_sc, l_sc, acc_sc = refs[at + len(outs) :]
    grp = HEADS // KV_HEADS
    tok = q_ref.shape[0]
    scale = HEAD_DIM ** (-0.5)

    for g in range(KV_HEADS):
        for j in range(grp):
            col = (g * grp + j) * HEAD_DIM
            qs_sc[g, :, j * tok : (j + 1) * tok] = q_ref[:, col : col + HEAD_DIM].T
    if first:
        m_sc[...] = jnp.full_like(m_sc, NEG)
        l_sc[...] = jnp.zeros_like(l_sc)
        acc_sc[...] = jnp.zeros_like(acc_sc)
    else:
        m_sc[...] = m_in[...]
        l_sc[...] = l_in[...]
        acc_sc[...] = acc_in[...]

    def update(kv_ref, masked):
        def one(g, carry):
            k = kv_ref[g]
            v = kv_ref[KV_HEADS + g]
            s = jnp.dot(k, qs_sc[g], preferred_element_type=jnp.float32) * scale
            if masked:
                rows = lax.broadcasted_iota(jnp.int32, s.shape, 0)
                cols = lax.broadcasted_iota(jnp.int32, s.shape, 1) % tok
                s = jnp.where(rows <= cols, s, NEG)
            m_old = m_sc[g]
            m_new = jnp.maximum(m_old, jnp.max(s, axis=0, keepdims=True))
            p = jnp.exp(s - m_new)
            alpha = jnp.exp(m_old - m_new)
            l_sc[g] = alpha * l_sc[g] + jnp.sum(p, axis=0, keepdims=True)
            pv = lax.dot_general(
                v, p.astype(jnp.bfloat16), (((0,), (0,)), ((), ())),
                preferred_element_type=jnp.float32,
            )
            acc_sc[g] = alpha * acc_sc[g] + pv
            m_sc[g] = m_new
            return carry

        lax.fori_loop(0, KV_HEADS, one, 0)

    for i in range(count):
        if first and i == 0:
            update(kv_refs[0], True)
            continue

        @pl.when(flags_ref[i] > 0)
        def _(i=i):
            update(kv_refs[i], False)

    if final:
        o_ref = outs[0]
        for g in range(KV_HEADS):
            normed = acc_sc[g] / l_sc[g]
            for j in range(grp):
                col = (g * grp + j) * HEAD_DIM
                o_ref[:, col : col + HEAD_DIM] = normed[:, j * tok : (j + 1) * tok].T
    else:
        outs[0][...] = m_sc[...]
        outs[1][...] = l_sc[...]
        outs[2][...] = acc_sc[...]


def flash(flags, query, blocks, state, final):
    tok = query.shape[0]
    grp = HEADS // KV_HEADS
    vmem = pl.BlockSpec(memory_space=pltpu.VMEM)
    stat = jax.ShapeDtypeStruct((KV_HEADS, 1, grp * tok), jnp.float32)
    acc = jax.ShapeDtypeStruct((KV_HEADS, HEAD_DIM, grp * tok), jnp.float32)
    if final:
        out_shape = jax.ShapeDtypeStruct((tok, HEADS * HEAD_DIM), jnp.float32)
        out_specs = vmem
    else:
        out_shape = (stat, stat, acc)
        out_specs = (vmem, vmem, vmem)
    first = state is None
    extra = () if first else tuple(state)
    kernel = functools.partial(flash_kernel, first, final, len(blocks))
    return pl.pallas_call(
        kernel,
        out_shape=out_shape,
        in_specs=[pl.BlockSpec(memory_space=pltpu.SMEM)]
        + [vmem] * (1 + len(extra) + len(blocks)),
        out_specs=out_specs,
        scratch_shapes=[
            pltpu.VMEM((KV_HEADS, HEAD_DIM, grp * tok), jnp.bfloat16),
            pltpu.VMEM((KV_HEADS, 1, grp * tok), jnp.float32),
            pltpu.VMEM((KV_HEADS, 1, grp * tok), jnp.float32),
            pltpu.VMEM((KV_HEADS, HEAD_DIM, grp * tok), jnp.float32),
        ],
        compiler_params=pltpu.CompilerParams(vmem_limit_bytes=48 * 1024 * 1024),
    )(flags, query, *extra, *blocks)


def attention(query, key_rows, val_rows, tok, ctx_index):
    count = lax.axis_size("ctx")
    rows = count // ROW
    kv = jnp.concatenate([key_rows, val_rows], axis=1)
    kv = kv.reshape(tok, 2 * KV_HEADS, HEAD_DIM).transpose(1, 0, 2)
    plus = [(r * ROW + z, r * ROW + (z + 1) % ROW) for r in range(rows) for z in range(ROW)]
    minus = [(r * ROW + z, r * ROW + (z - 1) % ROW) for r in range(rows) for z in range(ROW)]
    lefts, rights = [kv], [kv]
    lefts.append(lax.ppermute(kv, "ctx", plus))
    rights.append(lax.ppermute(kv, "ctx", minus))
    for _ in range(ROW // 2 - 1):
        lefts.append(lax.ppermute(lefts[-1], "ctx", plus))
    for _ in range(ROW - 2 - ROW // 2):
        rights.append(lax.ppermute(rights[-1], "ctx", minus))
    row_blocks = [kv]
    for k in range(1, max(len(lefts), len(rights))):
        row_blocks += [side[k] for side in (lefts, rights) if k < len(side)]
    z = ctx_index % ROW
    r = ctx_index // ROW
    flags = [jnp.int32(1)]
    for k in range(1, max(len(lefts), len(rights))):
        if k < len(lefts):
            flags.append((z - k >= 0).astype(jnp.int32))
        if k < len(rights):
            flags.append((z + k >= ROW).astype(jnp.int32))
    blocks = list(row_blocks)
    for lower in range(rows - 1):
        for upper in range(lower + 1, rows):
            up = [(lower * ROW + z2, upper * ROW + z2) for z2 in range(ROW)]
            for piece in row_blocks:
                blocks.append(lax.ppermute(piece, "ctx", up))
                flags.append((r == upper).astype(jnp.int32))
    split = len(row_blocks)
    if split == len(blocks):
        return flash(jnp.stack(flags), query, blocks, None, True)
    state = flash(jnp.stack(flags[:3]), query, blocks[:3], None, False)
    state = flash(jnp.stack(flags[3:split]), query, blocks[3:split], state, False)
    late = split + len(row_blocks) - 3
    last = len(blocks) - 1
    state = flash(jnp.stack(flags[split:late]), query, blocks[split:late], state, False)
    state = flash(jnp.stack(flags[late:last]), query, blocks[late:last], state, False)
    return flash(jnp.stack(flags[last:]), query, blocks[last:], state, True)


def hyena_conv(first_in, value_in, filters, tok):
    width = first_in.shape[1]
    taps = filters.shape[1]
    fgroups = filters.shape[0]
    lower, upper = circulant_parts(filters, taps)
    u_rows = (first_in.astype(jnp.float32) * value_in.astype(jnp.float32)).astype(jnp.bfloat16)
    before = passed_along(u_rows[tok - taps :], "ctx", 1)
    return conv_body(before, u_rows, lower, upper, tok, width, taps, fgroups)


def circulant_parts(filters, taps):
    rows_at = jnp.arange(taps, dtype=jnp.int32)
    lag = rows_at[:, None] - rows_at[None, :]
    wrapped = (lag + taps) % taps
    selector = (wrapped[None, :, :] == rows_at[:, None, None]).astype(jnp.bfloat16)
    circulant = jnp.einsum(
        "gk,kij->gij", filters, selector, preferred_element_type=jnp.float32
    ).astype(jnp.bfloat16)
    nothing = jnp.zeros((), jnp.bfloat16)
    lower = jnp.where((lag >= 0)[None], circulant, nothing)
    upper = jnp.where((lag < 0)[None], circulant, nothing)
    return lower, upper


def conv_body(before, u_rows, lower, upper, tok, width, taps, fgroups):
    extended = jnp.concatenate([before, u_rows], 0)
    nblk = tok // taps
    blocks = extended.reshape(nblk + 1, taps, fgroups, width // fgroups)
    conv = jnp.einsum("gij,bjgc->bigc", lower, blocks[1:], preferred_element_type=jnp.float32)
    conv = conv + jnp.einsum(
        "gij,bjgc->bigc", upper, blocks[:-1], preferred_element_type=jnp.float32
    )
    return conv.reshape(tok, width)


def blend(rows, width):
    gates = rows[:, :width].astype(jnp.float32)
    vals = rows[:, width:].astype(jnp.float32)
    return (jax.nn.sigmoid(gates) * vals).astype(jnp.bfloat16)


def place_rows(slots, rows, total_slots):
    placing = (jnp.arange(total_slots, dtype=jnp.int32)[:, None] == slots[None, :]).astype(
        jnp.bfloat16
    )
    return jnp.dot(placing, rows, preferred_element_type=jnp.float32).astype(jnp.bfloat16)


def route_hints(panels, owner, step_rows, width, tok, ctx_index):
    dp_count = lax.axis_size("dp")
    count = panels.shape[1]
    entries = panels.shape[2]
    cap = min(count, 4 * count // dp_count)
    owners = owner[0, :, 0]
    marks = (owners[:, None] == jnp.arange(dp_count, dtype=jnp.int32)[None, :]).astype(jnp.int32)
    before_mask = (
        jnp.arange(count, dtype=jnp.int32)[:, None] > jnp.arange(count, dtype=jnp.int32)[None, :]
    ).astype(jnp.int32)
    earlier = jnp.sum(jnp.dot(before_mask, marks) * marks, axis=1)
    slots = owners * cap + earlier
    base_row = ctx_index * tok
    offsets = (step_rows[0] - base_row).astype(jnp.bfloat16)
    lanes = jnp.arange(128, dtype=jnp.int32)[None, :] == 0
    offset_cols = jnp.where(lanes, offsets[:, None], jnp.zeros((), jnp.bfloat16))
    rows_ext = jnp.concatenate([panels[0], offset_cols], axis=1)
    buffer = place_rows(slots, rows_ext, dp_count * cap)
    received = lax.all_to_all(
        buffer.reshape(dp_count, cap, entries + 128), "dp", split_axis=0, concat_axis=0, tiled=True
    ).reshape(dp_count * cap, entries + 128)
    arrived_rows = received[:, entries].astype(jnp.int32)
    arrived = blend(received[:, :entries], width)
    landing = (jnp.arange(tok, dtype=jnp.int32)[:, None] == arrived_rows[None, :]).astype(
        jnp.bfloat16
    )
    return jnp.dot(landing, arrived, preferred_element_type=jnp.float32)


def per_device(
    queries, keys, values, hyena_x1, hyena_x2, hyena_v, filters, panels, owner, step_rows
):
    tok = queries.shape[1]
    width = hyena_x1.shape[2]
    ctx_index = lax.axis_index("ctx")
    conv = hyena_conv(hyena_x1[0], hyena_v[0], filters, tok)
    attended = attention(queries[0], keys[0], values[0], tok, ctx_index)
    hints = route_hints(panels, owner, step_rows, width, tok, ctx_index)
    total = hyena_x2[0].astype(jnp.float32) * conv + attended + hints
    return total.astype(jnp.bfloat16)[None]


def solution(mesh):
    placed = (
        P("dp", "ctx", None),
        P("dp", "ctx", None),
        P("dp", "ctx", None),
        P("dp", "ctx", None),
        P("dp", "ctx", None),
        P("dp", "ctx", None),
        P(),
        P("dp", "ctx", None),
        P("dp", "ctx", None),
        P("dp", "ctx"),
    )
    return jax.shard_map(
        per_device, mesh=mesh, in_specs=placed, out_specs=P("dp", "ctx", None), check_vma=False
    )
```
